1024 devices in a mesh: pipe: 16 (over x_hi, y), expert: 8 (over x_lo, core), dp: 8 (over z).
Axes of the slice: x: 8 (x_hi: 2, x_lo: 4; x = x_hi * 4 + x_lo), y: 8, z: 8, core: 2. Of those that a mesh axis runs over, the one named last changes fastest.
Arguments:
- tokens: bfloat16 [1536, 6144], P('expert', 'dp'), may hold values from -6 to 6
- expert_ids: int32 [1536, 2], P('expert'), may hold values from 0 to 7, all different within a row; in each aligned block of 192 rows (0 to 191, 192 to 383, ...) at most 60 rows name the same one
- gate_share: float32 [1536, 2], P('expert'), may hold values from 0.1 to 1
- gate_proj: bfloat16 [8, 6144, 8192], P('expert', 'dp', 'pipe'), may hold values from -0.078125 to 0.078125
- up_proj: bfloat16 [8, 6144, 8192], P('expert', 'dp', 'pipe'), may hold values from -0.078125 to 0.078125
- down_proj: bfloat16 [8, 8192, 6144], P('expert', 'pipe', 'dp'), may hold values from -0.0625 to 0.0625
Outputs:
- layer_out: bfloat16 [1536, 6144], P('expert', 'dp')
The draws below stay inside these ranges and needn't reach their ends.
Inputs may be any that keep to these rules, and one draw needn't show every extreme that they name: `expert_ids`: each token names two different experts. Among the 192 tokens of one source block, no expert is named by more than 60 of them, and in every draw some expert is named by exactly 60 in some block.
All inputs are finite; a program needn't handle non-finite values.
Results may differ from the reference program's by a relative error of at most 0.0049.
Values may be sent and summed in bfloat16 or wider, within the bound.
No kernel may reach another device: no remote copies, remote signals or barrier semaphores. Data moves between devices by JAX's collectives and lax.ppermute only.
A program may use at most 32 MiB of HBM per device.

```python
import math
import jax
import jax.numpy as jnp
import numpy as np
from jax import lax

D = 6144
FF = 8192
TOK_DEV = 192
EXPERTS = 8
CAP = 60
TOKENS = 1536
N_EXPERT = 8


def shard_levels(stream_key, extent, shards, least, largest):
    def one(position, shards_of):
        draws = jax.random.uniform(jax.random.fold_in(jax.random.fold_in(stream_key, 6), position), (shards_of,), jnp.float32, least / len(shards), largest / len(shards))
        return jnp.repeat(jnp.exp(draws), extent[position] // shards_of).reshape((-1,) + (1,) * (len(extent) - position - 1))

    gain = one(*shards[0])
    for cut in shards[1:]:
        gain = gain * one(*cut)
    return gain


def shared_out(stream_key, own, number, rows, amount, top, bound, slope):
    order = jax.random.permutation(stream_key, amount)
    packed, common = shares(amount, rows * top, bound, slope, True), shares(amount, rows * top, bound, slope, False)
    places = jnp.arange(amount)

    def named(lengths, rotation):
        used = int((lengths > 0).sum())
        fixed = max(1, used // 4)
        shifted = fixed + (places - fixed + rotation * (used - fixed)) % max(1, amount - fixed)
        return jnp.zeros((amount,), jnp.int32).at[order[jnp.where(places < fixed, places, shifted)]].set(jnp.asarray(lengths, jnp.int32))

    lengths = jnp.where(number % 4 == 0, named(packed, number // 4), named(common, number - number // 4 - 1))
    mixed = jax.random.permutation(jax.random.fold_in(own, 3), amount)
    giver, sink = mixed[0:amount // 2 * 2:2], mixed[1:amount // 2 * 2:2]
    slack = jnp.minimum(lengths[giver] - 1, bound - lengths[sink]) // 2
    slack = jnp.where((giver == order[0]) | (sink == order[0]) | (lengths[sink] == 0), 0, jnp.maximum(slack, 0))
    shifted = jax.random.randint(jax.random.fold_in(own, 4), (amount // 2,), 0, 1 << 20) % (slack + 1)
    lengths = lengths.at[giver].add(-shifted).at[sink].add(shifted)
    items = jnp.searchsorted(jnp.cumsum(lengths), jnp.arange(rows * top), side="right").astype(jnp.int32)
    table = items.reshape(top, rows).T
    table = table[jax.random.permutation(jax.random.fold_in(own, 1), rows)]
    rotation = jax.random.randint(jax.random.fold_in(own, 2), (rows, 1), 0, top)
    return jnp.take_along_axis(table, (jnp.arange(top)[None, :] + rotation) % top, axis=1)


def shares(amount, total, most, slope, full):
    portions = [(1 << 20) // math.isqrt(grade ** slope) + 1 for grade in range(1, amount + 1)]
    largest = most if full else min(most, max(-(-total // amount), total * portions[0] // sum(portions)))
    least = 1 if total - largest >= amount - 1 else 0
    given, surplus = [largest] + [least] * (amount - 1), total - largest - least * (amount - 1)
    while surplus > 0:
        movable = [i for i in range(1, amount) if given[i] < largest] or [i for i in range(1, amount) if given[i] < most]
        whole, left = sum([portions[i] for i in movable]), surplus
        for i in movable:
            extra = min(most - given[i], max(1, left * portions[i] // whole), surplus)
            given[i] = given[i] + extra
            surplus = surplus - extra
    return np.array(given)


def centred(own_key, dims, spread, bound, pieces=(), held_as=jnp.bfloat16):
    loudness = shard_levels(own_key, dims, pieces, -0.22, 0.18) if pieces else 1.0
    values = jax.random.normal(own_key, dims, jnp.float32) * spread * loudness
    return jnp.minimum(jnp.maximum(values, -bound), bound).astype(held_as)


def setup_inputs(seed: int = 0) -> dict:
    splits = jax.random.split(jax.random.key(seed), 7)
    tokens = centred(splits[0], (TOKENS, D), 1.0, 6.0, ((0, 8), (1, 8)))
    expert_ids_keys = jax.random.split(jax.random.fold_in(splits[1], 1), TOKENS // TOK_DEV)
    expert_ids_turns = jax.random.permutation(jax.random.fold_in(splits[1], 3), TOKENS // TOK_DEV)
    expert_ids = jax.vmap(lambda own, number: shared_out(jax.random.fold_in(splits[1], 2), own, number, TOK_DEV, EXPERTS, 2, CAP, 2))(expert_ids_keys, expert_ids_turns).reshape((TOKENS, 2))
    gate_share = jnp.clip(0.1 + 0.9 * jax.random.uniform(splits[2], (TOKENS, 2), jnp.float32) ** shard_levels(splits[2], (TOKENS, 2), ((0, 8),), -0.2, 0.2), 0.1, 1.0)
    gate_proj = centred(splits[3], (EXPERTS, D, FF), D ** -0.5, 0.078125, ((0, 8), (1, 8), (2, 16)))
    up_proj = centred(splits[4], (EXPERTS, D, FF), D ** -0.5, 0.078125, ((0, 8), (1, 8), (2, 16)))
    down_proj = centred(splits[5], (EXPERTS, FF, D), FF ** -0.5, 0.0625, ((0, 8), (1, 16), (2, 8)))
    return dict(tokens=tokens, expert_ids=expert_ids, gate_share=gate_share, gate_proj=gate_proj, up_proj=up_proj, down_proj=down_proj)


def slot_targets(expert_ids):
    blocks = expert_ids.reshape(N_EXPERT, TOK_DEV * 2)
    onehot = (blocks[:, :, None] == jnp.arange(EXPERTS, dtype=jnp.int32)[None, None, :]).astype(jnp.int32)
    before = jnp.cumsum(onehot, axis=1) - onehot
    slot_rank = jnp.sum(before * onehot, axis=2)
    source = jnp.arange(N_EXPERT, dtype=jnp.int32)[:, None]
    target = blocks * (N_EXPERT * CAP) + source * CAP + slot_rank
    return target.reshape(TOKENS, 2).astype(jnp.int32)


def reference(tokens, expert_ids, gate_share, gate_proj, up_proj, down_proj):
    target = slot_targets(expert_ids)
    slot_count = EXPERTS * N_EXPERT * CAP
    owners = (jnp.arange(TOKENS * 2, dtype=jnp.int32) // 2 + 1).astype(jnp.int32)
    slot_table = jnp.zeros((slot_count,), jnp.int32).at[target.reshape(-1)].set(owners)
    slot_table = slot_table.reshape(EXPERTS, N_EXPERT * CAP)

    def expert_apply(index):
        row_ids = slot_table[index]
        filled = row_ids > 0
        safe_ids = jnp.maximum(row_ids - 1, 0).astype(jnp.int32)
        inputs = jnp.where(filled[:, None], tokens[safe_ids], jnp.zeros((), jnp.bfloat16))
        gate_val = jnp.dot(inputs, gate_proj[index], preferred_element_type=jnp.float32)
        up_val = jnp.dot(inputs, up_proj[index], preferred_element_type=jnp.float32)
        hidden = (jax.nn.silu(gate_val) * up_val).astype(jnp.bfloat16)
        return jnp.dot(hidden, down_proj[index], preferred_element_type=jnp.float32)

    expert_rows = lax.map(expert_apply, jnp.arange(EXPERTS, dtype=jnp.int32))
    flattened = expert_rows.reshape(slot_count, D)
    picked = flattened[target]
    layer_out = jnp.sum(gate_share[:, :, None].astype(jnp.float32) * picked, axis=1)
    return layer_out.astype(jnp.bfloat16)
```

```python
import jax
import jax.numpy as jnp
from jax import lax
from jax.sharding import PartitionSpec as P


def swiglu(gate_up):
    middle = gate_up.shape[1] // 2
    return (jax.nn.silu(gate_up[:, :middle]) * gate_up[:, middle:]).astype(jnp.bfloat16)


def gather_rows(part, axis):
    count = lax.axis_size(axis)
    copies = jnp.broadcast_to(part[None], (count,) + part.shape)
    gathered = lax.all_to_all(copies, axis, split_axis=0, concat_axis=0, tiled=True)
    return gathered.reshape((count * part.shape[0],) + part.shape[1:])


def body(tokens, expert_ids, gate_share, gate_proj, up_proj, down_proj):
    tok_rows = tokens.shape[0]
    columns = tokens.shape[1]
    groups = lax.axis_size("expert")
    n_pipe = lax.axis_size("pipe")
    capacity = min(tok_rows, 5 * tok_rows // (2 * groups))
    slots_all = groups * capacity
    choices_flat = expert_ids.reshape(-1)
    onehot = (choices_flat[:, None] == jnp.arange(groups, dtype=jnp.int32)[None, :]).astype(
        jnp.int32
    )
    before = jnp.cumsum(onehot, axis=0) - onehot
    slot_rank = jnp.sum(before * onehot, axis=1)
    target = choices_flat * capacity + slot_rank
    placed = (target[:, None] == jnp.arange(slots_all, dtype=jnp.int32)[None, :]).reshape(
        tok_rows, 2, slots_all
    )
    dispatch_map = jnp.sum(placed.astype(jnp.bfloat16), axis=1)
    weighting = jnp.sum(placed.astype(jnp.float32) * gate_share[:, :, None], axis=1)
    outbound = lax.dot_general(
        dispatch_map, tokens, (((0,), (0,)), ((), ())), preferred_element_type=jnp.float32
    )
    outbound = outbound.astype(jnp.bfloat16).reshape(groups, capacity, columns)
    received = lax.all_to_all(outbound, "expert", split_axis=0, concat_axis=0, tiled=True).reshape(
        slots_all, columns
    )
    gate_part = jnp.dot(received, gate_proj[0], preferred_element_type=jnp.float32)
    up_part = jnp.dot(received, up_proj[0], preferred_element_type=jnp.float32)
    gate_up = jnp.concatenate([gate_part, up_part], axis=1)
    n_dp = lax.axis_size("dp")
    summed = jnp.sum(
        lax.all_to_all(
            gate_up.reshape(n_dp, slots_all // n_dp, -1), "dp", split_axis=0, concat_axis=0, tiled=True
        ),
        axis=0,
    )
    hidden = gather_rows(swiglu(summed), "dp")
    expert_part = jnp.dot(hidden, down_proj[0], preferred_element_type=jnp.float32)
    returned = lax.all_to_all(
        expert_part.reshape(groups, capacity, columns),
        "expert",
        split_axis=0,
        concat_axis=0,
        tiled=True,
    ).reshape(slots_all, columns)
    combined = lax.dot_general(
        weighting,
        returned,
        (((1,), (0,)), ((), ())),
        precision=lax.Precision.HIGHEST,
        preferred_element_type=jnp.float32,
    )
    share = jnp.sum(
        lax.all_to_all(
            combined.reshape(n_pipe, tok_rows // n_pipe, columns),
            "pipe",
            split_axis=0,
            concat_axis=0,
            tiled=True,
        ),
        axis=0,
    )
    return gather_rows(share.astype(jnp.bfloat16), "pipe")


def solution(mesh):
    return jax.shard_map(
        body,
        mesh=mesh,
        in_specs=(
            P("expert", "dp"),
            P("expert", None),
            P("expert", None),
            P("expert", "dp", "pipe"),
            P("expert", "dp", "pipe"),
            P("expert", "pipe", "dp"),
        ),
        out_specs=P("expert", "dp"),
        check_vma=False,
    )
```

```python
import jax
import jax.numpy as jnp
from jax import lax
from jax.sharding import PartitionSpec as P


def swiglu(gate_up):
    middle = gate_up.shape[1] // 2
    return (jax.nn.silu(gate_up[:, :middle]) * gate_up[:, middle:]).astype(jnp.bfloat16)


def gather_rows(part, axis):
    count = lax.axis_size(axis)
    copies = jnp.broadcast_to(part[None], (count,) + part.shape)
    gathered = lax.all_to_all(copies, axis, split_axis=0, concat_axis=0, tiled=True)
    return gathered.reshape((count * part.shape[0],) + part.shape[1:])


def body(tokens, expert_ids, gate_share, gate_proj, up_proj, down_proj):
    tok_rows = tokens.shape[0]
    columns = tokens.shape[1]
    groups = lax.axis_size("expert")
    n_pipe = lax.axis_size("pipe")
    capacity = min(tok_rows, 5 * tok_rows // (2 * groups))
    slots_all = groups * capacity
    choices_flat = expert_ids.reshape(-1)
    onehot = (choices_flat[:, None] == jnp.arange(groups, dtype=jnp.int32)[None, :]).astype(
        jnp.int32
    )
    before = jnp.cumsum(onehot, axis=0) - onehot
    slot_rank = jnp.sum(before * onehot, axis=1)
    target = choices_flat * capacity + slot_rank
    placed = (target[:, None] == jnp.arange(slots_all, dtype=jnp.int32)[None, :]).reshape(
        tok_rows, 2, slots_all
    )
    dispatch_map = jnp.sum(placed.astype(jnp.bfloat16), axis=1)
    weighting = jnp.sum(placed.astype(jnp.float32) * gate_share[:, :, None], axis=1)
    outbound = lax.dot_general(
        dispatch_map, tokens, (((0,), (0,)), ((), ())), preferred_element_type=jnp.float32
    )
    outbound = outbound.astype(jnp.bfloat16).reshape(groups, capacity, columns)
    received = lax.all_to_all(outbound, "expert", split_axis=0, concat_axis=0, tiled=True).reshape(
        slots_all, columns
    )
    gate_part = jnp.dot(received, gate_proj[0], preferred_element_type=jnp.float32)
    up_part = jnp.dot(received, up_proj[0], preferred_element_type=jnp.float32)
    gate_up = jnp.concatenate([gate_part, up_part], axis=1)
    n_dp = lax.axis_size("dp")
    summed = jnp.sum(
        lax.all_to_all(
            gate_up.reshape(n_dp, slots_all // n_dp, -1), "dp", split_axis=0, concat_axis=0, tiled=True
        ),
        axis=0,
    )
    hidden = gather_rows(swiglu(summed), "dp")
    expert_part = jnp.dot(hidden, down_proj[0], preferred_element_type=jnp.float32)
    returned = lax.all_to_all(
        expert_part.astype(jnp.bfloat16).reshape(groups, capacity, columns),
        "expert",
        split_axis=0,
        concat_axis=0,
        tiled=True,
    ).reshape(slots_all, columns)
    combined = lax.dot_general(
        weighting,
        returned.astype(jnp.float32),
        (((1,), (0,)), ((), ())),
        precision=lax.Precision.HIGHEST,
        preferred_element_type=jnp.float32,
    )
    share = jnp.sum(
        lax.all_to_all(
            combined.reshape(n_pipe, tok_rows // n_pipe, columns),
            "pipe",
            split_axis=0,
            concat_axis=0,
            tiled=True,
        ),
        axis=0,
    )
    return gather_rows(share.astype(jnp.bfloat16), "pipe")


def solution(mesh):
    return jax.shard_map(
        body,
        mesh=mesh,
        in_specs=(
            P("expert", "dp"),
            P("expert", None),
            P("expert", None),
            P("expert", "dp", "pipe"),
            P("expert", "dp", "pipe"),
            P("expert", "pipe", "dp"),
        ),
        out_specs=P("expert", "dp"),
        check_vma=False,
    )
```

```python
import jax
import jax.numpy as jnp
from jax import lax
from jax.sharding import PartitionSpec as P


def swiglu(gate_up):
    middle = gate_up.shape[1] // 2
    return (jax.nn.silu(gate_up[:, :middle]) * gate_up[:, middle:]).astype(jnp.bfloat16)


def gather_rows(part, axis):
    count = lax.axis_size(axis)
    copies = jnp.broadcast_to(part[None], (count,) + part.shape)
    gathered = lax.all_to_all(copies, axis, split_axis=0, concat_axis=0, tiled=True)
    return gathered.reshape((count * part.shape[0],) + part.shape[1:])


def body(tokens, expert_ids, gate_share, gate_proj, up_proj, down_proj):
    tok_rows = tokens.shape[0]
    columns = tokens.shape[1]
    groups = lax.axis_size("expert")
    n_pipe = lax.axis_size("pipe")
    capacity = min(tok_rows, 5 * tok_rows // (2 * groups))
    slots_all = groups * capacity
    choices_flat = expert_ids.reshape(-1)
    onehot = (choices_flat[:, None] == jnp.arange(groups, dtype=jnp.int32)[None, :]).astype(
        jnp.int32
    )
    before = jnp.cumsum(onehot, axis=0) - onehot
    slot_rank = jnp.sum(before * onehot, axis=1)
    target = choices_flat * capacity + slot_rank
    placed = (target[:, None] == jnp.arange(slots_all, dtype=jnp.int32)[None, :]).reshape(
        tok_rows, 2, slots_all
    )
    dispatch_map = jnp.sum(placed.astype(jnp.bfloat16), axis=1)
    weighting = jnp.sum(placed.astype(jnp.float32) * gate_share[:, :, None], axis=1)
    outbound = lax.dot_general(
        dispatch_map, tokens, (((0,), (0,)), ((), ())), preferred_element_type=jnp.float32
    )
    outbound = outbound.astype(jnp.bfloat16).reshape(groups, capacity, columns)
    received = lax.all_to_all(outbound, "expert", split_axis=0, concat_axis=0, tiled=True).reshape(
        slots_all, columns
    )
    gate_part = jnp.dot(received, gate_proj[0], preferred_element_type=jnp.float32)
    up_part = jnp.dot(received, up_proj[0], preferred_element_type=jnp.float32)
    gate_up = jnp.concatenate([gate_part, up_part], axis=1)
    summed = lax.psum_scatter(gate_up, "dp", scatter_dimension=0, tiled=True)
    summed = lax.optimization_barrier(summed)
    hidden = gather_rows(swiglu(summed), "dp")
    expert_part = jnp.dot(hidden, down_proj[0], preferred_element_type=jnp.float32)
    returned = lax.all_to_all(
        expert_part.astype(jnp.bfloat16).reshape(groups, capacity, columns),
        "expert",
        split_axis=0,
        concat_axis=0,
        tiled=True,
    ).reshape(slots_all, columns)
    combined = lax.dot_general(
        weighting,
        returned.astype(jnp.float32),
        (((1,), (0,)), ((), ())),
        precision=lax.Precision.HIGHEST,
        preferred_element_type=jnp.float32,
    )
    share = jnp.sum(
        lax.all_to_all(
            combined.reshape(n_pipe, tok_rows // n_pipe, columns),
            "pipe",
            split_axis=0,
            concat_axis=0,
            tiled=True,
        ),
        axis=0,
    )
    return gather_rows(share.astype(jnp.bfloat16), "pipe")


def solution(mesh):
    return jax.shard_map(
        body,
        mesh=mesh,
        in_specs=(
            P("expert", "dp"),
            P("expert", None),
            P("expert", None),
            P("expert", "dp", "pipe"),
            P("expert", "dp", "pipe"),
            P("expert", "pipe", "dp"),
        ),
        out_specs=P("expert", "dp"),
        check_vma=False,
    )
```

```python
import jax
import jax.numpy as jnp
from jax import lax
from jax.sharding import PartitionSpec as P


def swiglu(gate_up):
    middle = gate_up.shape[1] // 2
    return (jax.nn.silu(gate_up[:, :middle]) * gate_up[:, middle:]).astype(jnp.bfloat16)


def gather_rows(part, axis):
    count = lax.axis_size(axis)
    me = lax.axis_index(axis)
    gathered = jnp.zeros((count,) + part.shape, part.dtype)
    gathered = lax.dynamic_update_index_in_dim(gathered, part, me, 0)
    for shift in range(1, count):
        got = lax.ppermute(part, axis, [(i, (i + shift) % count) for i in range(count)])
        gathered = lax.dynamic_update_index_in_dim(gathered, got, (me + count - shift) % count, 0)
    return gathered.reshape((count * part.shape[0],) + part.shape[1:])


def body(tokens, expert_ids, gate_share, gate_proj, up_proj, down_proj):
    tok_rows = tokens.shape[0]
    columns = tokens.shape[1]
    groups = lax.axis_size("expert")
    n_pipe = lax.axis_size("pipe")
    capacity = min(tok_rows, 5 * tok_rows // (2 * groups))
    slots_all = groups * capacity
    choices_flat = expert_ids.reshape(-1)
    onehot = (choices_flat[:, None] == jnp.arange(groups, dtype=jnp.int32)[None, :]).astype(
        jnp.int32
    )
    before = jnp.cumsum(onehot, axis=0) - onehot
    slot_rank = jnp.sum(before * onehot, axis=1)
    target = choices_flat * capacity + slot_rank
    placed = (target[:, None] == jnp.arange(slots_all, dtype=jnp.int32)[None, :]).reshape(
        tok_rows, 2, slots_all
    )
    dispatch_map = jnp.sum(placed.astype(jnp.bfloat16), axis=1)
    weighting = jnp.sum(placed.astype(jnp.float32) * gate_share[:, :, None], axis=1)
    outbound = lax.dot_general(
        dispatch_map, tokens, (((0,), (0,)), ((), ())), preferred_element_type=jnp.float32
    )
    outbound = outbound.astype(jnp.bfloat16).reshape(groups, capacity, columns)
    received = lax.all_to_all(outbound, "expert", split_axis=0, concat_axis=0, tiled=True).reshape(
        slots_all, columns
    )
    gate_part = jnp.dot(received, gate_proj[0], preferred_element_type=jnp.float32)
    up_part = jnp.dot(received, up_proj[0], preferred_element_type=jnp.float32)
    gate_up = jnp.concatenate([gate_part, up_part], axis=1)
    summed = lax.psum_scatter(gate_up, "dp", scatter_dimension=0, tiled=True)
    summed = lax.optimization_barrier(summed)
    hidden = gather_rows(swiglu(summed), "dp")
    expert_part = jnp.dot(hidden, down_proj[0], preferred_element_type=jnp.float32)
    returned = lax.all_to_all(
        expert_part.astype(jnp.bfloat16).reshape(groups, capacity, columns),
        "expert",
        split_axis=0,
        concat_axis=0,
        tiled=True,
    ).reshape(slots_all, columns)
    combined = lax.dot_general(
        weighting,
        returned.astype(jnp.float32),
        (((1,), (0,)), ((), ())),
        precision=lax.Precision.HIGHEST,
        preferred_element_type=jnp.float32,
    )
    share = jnp.sum(
        lax.all_to_all(
            combined.reshape(n_pipe, tok_rows // n_pipe, columns),
            "pipe",
            split_axis=0,
            concat_axis=0,
            tiled=True,
        ),
        axis=0,
    )
    return gather_rows(share.astype(jnp.bfloat16), "pipe")


def solution(mesh):
    return jax.shard_map(
        body,
        mesh=mesh,
        in_specs=(
            P("expert", "dp"),
            P("expert", None),
            P("expert", None),
            P("expert", "dp", "pipe"),
            P("expert", "dp", "pipe"),
            P("expert", "pipe", "dp"),
        ),
        out_specs=P("expert", "dp"),
        check_vma=False,
    )
```

```python
import jax
import jax.numpy as jnp
from jax import lax
from jax.sharding import PartitionSpec as P


def swiglu(gate_up):
    middle = gate_up.shape[1] // 2
    return (jax.nn.silu(gate_up[:, :middle]) * gate_up[:, middle:]).astype(jnp.bfloat16)


def gather_rows(part, axis):
    count = lax.axis_size(axis)
    copies = jnp.broadcast_to(part[None], (count,) + part.shape)
    gathered = lax.all_to_all(copies, axis, split_axis=0, concat_axis=0, tiled=True)
    return gathered.reshape((count * part.shape[0],) + part.shape[1:])


def body(tokens, expert_ids, gate_share, gate_proj, up_proj, down_proj):
    tok_rows = tokens.shape[0]
    columns = tokens.shape[1]
    groups = lax.axis_size("expert")
    n_pipe = lax.axis_size("pipe")
    capacity = min(tok_rows, 5 * tok_rows // (2 * groups))
    slots_all = groups * capacity
    choices_flat = expert_ids.reshape(-1)
    onehot = (choices_flat[:, None] == jnp.arange(groups, dtype=jnp.int32)[None, :]).astype(
        jnp.int32
    )
    before = jnp.cumsum(onehot, axis=0) - onehot
    slot_rank = jnp.sum(before * onehot, axis=1)
    target = choices_flat * capacity + slot_rank
    placed = (target[:, None] == jnp.arange(slots_all, dtype=jnp.int32)[None, :]).reshape(
        tok_rows, 2, slots_all
    )
    dispatch_map = jnp.sum(placed.astype(jnp.bfloat16), axis=1)
    weighting = jnp.sum(placed.astype(jnp.float32) * gate_share[:, :, None], axis=1)
    outbound = lax.dot_general(
        dispatch_map, tokens, (((0,), (0,)), ((), ())), preferred_element_type=jnp.float32
    )
    outbound = outbound.astype(jnp.bfloat16).reshape(groups, capacity, columns)
    received = lax.all_to_all(outbound, "expert", split_axis=0, concat_axis=0, tiled=True).reshape(
        slots_all, columns
    )
    gate_part = jnp.dot(received, gate_proj[0], preferred_element_type=jnp.float32)
    up_part = jnp.dot(received, up_proj[0], preferred_element_type=jnp.float32)
    gate_up = jnp.concatenate([gate_part, up_part], axis=1)
    summed = lax.psum_scatter(gate_up, "dp", scatter_dimension=0, tiled=True)
    summed = lax.optimization_barrier(summed)
    hidden = gather_rows(swiglu(summed), "dp")
    expert_part = jnp.dot(hidden, down_proj[0], preferred_element_type=jnp.float32)
    width = columns // n_pipe
    outgoing = expert_part.astype(jnp.bfloat16).reshape(groups, capacity, n_pipe, width)
    outgoing = jnp.transpose(outgoing, (2, 0, 1, 3)).reshape(n_pipe * groups, capacity, width)
    arrived = lax.all_to_all(outgoing, ("pipe", "expert"), split_axis=0, concat_axis=0, tiled=True)
    returned = jnp.sum(
        arrived.reshape(n_pipe, slots_all, width).astype(jnp.float32), axis=0
    )
    combined = lax.dot_general(
        weighting,
        returned,
        (((1,), (0,)), ((), ())),
        precision=lax.Precision.HIGHEST,
        preferred_element_type=jnp.float32,
    )
    return gather_cols(combined.astype(jnp.bfloat16), "pipe")


def gather_cols(part, axis):
    count = lax.axis_size(axis)
    copies = jnp.broadcast_to(part[None], (count,) + part.shape)
    gathered = lax.all_to_all(copies, axis, split_axis=0, concat_axis=0, tiled=True)
    return jnp.transpose(gathered, (1, 0, 2)).reshape(part.shape[0], count * part.shape[1])

def solution(mesh):
    return jax.shard_map(
        body,
        mesh=mesh,
        in_specs=(
            P("expert", "dp"),
            P("expert", None),
            P("expert", None),
            P("expert", "dp", "pipe"),
            P("expert", "dp", "pipe"),
            P("expert", "pipe", "dp"),
        ),
        out_specs=P("expert", "dp"),
        check_vma=False,
    )
```

```python
import jax
import jax.numpy as jnp
from jax import lax
from jax.sharding import PartitionSpec as P


def swiglu(gate_up):
    middle = gate_up.shape[1] // 2
    return (jax.nn.silu(gate_up[:, :middle]) * gate_up[:, middle:]).astype(jnp.bfloat16)


def gather_rows(part, axis):
    count = lax.axis_size(axis)
    copies = jnp.broadcast_to(part[None], (count,) + part.shape)
    gathered = lax.all_to_all(copies, axis, split_axis=0, concat_axis=0, tiled=True)
    return gathered.reshape((count * part.shape[0],) + part.shape[1:])


def body(tokens, expert_ids, gate_share, gate_proj, up_proj, down_proj):
    tok_rows = tokens.shape[0]
    columns = tokens.shape[1]
    groups = lax.axis_size("expert")
    n_pipe = lax.axis_size("pipe")
    capacity = min(tok_rows, 5 * tok_rows // (2 * groups))
    slots_all = groups * capacity
    choices_flat = expert_ids.reshape(-1)
    onehot = (choices_flat[:, None] == jnp.arange(groups, dtype=jnp.int32)[None, :]).astype(
        jnp.int32
    )
    before = jnp.cumsum(onehot, axis=0) - onehot
    slot_rank = jnp.sum(before * onehot, axis=1)
    target = choices_flat * capacity + slot_rank
    placed = (target[:, None] == jnp.arange(slots_all, dtype=jnp.int32)[None, :]).reshape(
        tok_rows, 2, slots_all
    )
    dispatch_map = jnp.sum(placed.astype(jnp.bfloat16), axis=1)
    weighting = jnp.sum(placed.astype(jnp.float32) * gate_share[:, :, None], axis=1)
    outbound = lax.dot_general(
        dispatch_map, tokens, (((0,), (0,)), ((), ())), preferred_element_type=jnp.float32
    )
    outbound = outbound.astype(jnp.bfloat16).reshape(groups, capacity, columns)
    received = lax.all_to_all(outbound, "expert", split_axis=0, concat_axis=0, tiled=True).reshape(
        slots_all, columns
    )
    gate_part = jnp.dot(received, gate_proj[0], preferred_element_type=jnp.float32)
    up_part = jnp.dot(received, up_proj[0], preferred_element_type=jnp.float32)
    gate_up = jnp.concatenate([gate_part, up_part], axis=1)
    summed = lax.psum_scatter(gate_up, "dp", scatter_dimension=0, tiled=True)
    summed = lax.optimization_barrier(summed)
    hidden = gather_rows(swiglu(summed), "dp")
    expert_part = jnp.dot(hidden, down_proj[0], preferred_element_type=jnp.float32)
    width = columns // n_pipe
    outgoing = expert_part.astype(jnp.bfloat16).reshape(groups, capacity, n_pipe, width)
    outgoing = jnp.transpose(outgoing, (2, 0, 1, 3)).reshape(n_pipe * groups, capacity, width)
    arrived = lax.all_to_all(outgoing, ("pipe", "expert"), split_axis=0, concat_axis=0, tiled=True)
    returned = jnp.sum(
        arrived.reshape(n_pipe, groups, capacity, width).astype(jnp.float32), axis=0
    )
    combined = lax.dot_general(
        weighting.reshape(tok_rows, groups, capacity),
        returned,
        (((1, 2), (0, 1)), ((), ())),
        precision=lax.Precision.HIGHEST,
        preferred_element_type=jnp.float32,
    )
    return gather_cols(combined.astype(jnp.bfloat16), "pipe")


def gather_cols(part, axis):
    count = lax.axis_size(axis)
    copies = jnp.broadcast_to(part[None], (count,) + part.shape)
    gathered = lax.all_to_all(copies, axis, split_axis=0, concat_axis=0, tiled=True)
    return jnp.transpose(gathered, (1, 0, 2)).reshape(part.shape[0], count * part.shape[1])

def solution(mesh):
    return jax.shard_map(
        body,
        mesh=mesh,
        in_specs=(
            P("expert", "dp"),
            P("expert", None),
            P("expert", None),
            P("expert", "dp", "pipe"),
            P("expert", "dp", "pipe"),
            P("expert", "pipe", "dp"),
        ),
        out_specs=P("expert", "dp"),
        check_vma=False,
    )
```

```python
import jax
import jax.numpy as jnp
from jax import lax
from jax.sharding import PartitionSpec as P


def swiglu(gate_up):
    middle = gate_up.shape[1] // 2
    return (jax.nn.silu(gate_up[:, :middle]) * gate_up[:, middle:]).astype(jnp.bfloat16)


def gather_rows(part, axis):
    count = lax.axis_size(axis)
    copies = jnp.broadcast_to(part[None], (count,) + part.shape)
    gathered = lax.all_to_all(copies, axis, split_axis=0, concat_axis=0, tiled=True)
    return gathered.reshape((count * part.shape[0],) + part.shape[1:])


def body(tokens, expert_ids, gate_share, gate_proj, up_proj, down_proj):
    tok_rows = tokens.shape[0]
    columns = tokens.shape[1]
    groups = lax.axis_size("expert")
    n_pipe = lax.axis_size("pipe")
    capacity = min(tok_rows, 5 * tok_rows // (2 * groups))
    slots_all = groups * capacity
    choices_flat = expert_ids.reshape(-1)
    onehot = (choices_flat[:, None] == jnp.arange(groups, dtype=jnp.int32)[None, :]).astype(
        jnp.int32
    )
    before = jnp.cumsum(onehot, axis=0) - onehot
    slot_rank = jnp.sum(before * onehot, axis=1)
    target = choices_flat * capacity + slot_rank
    placed = (target[:, None] == jnp.arange(slots_all, dtype=jnp.int32)[None, :]).reshape(
        tok_rows, 2, slots_all
    )
    dispatch_map = jnp.sum(placed.astype(jnp.bfloat16), axis=1)
    weighting = jnp.sum(placed.astype(jnp.float32) * gate_share[:, :, None], axis=1)
    outbound = lax.dot_general(
        dispatch_map, tokens, (((0,), (0,)), ((), ())), preferred_element_type=jnp.float32
    )
    outbound = outbound.astype(jnp.bfloat16).reshape(groups, capacity, columns)
    received = lax.all_to_all(outbound, "expert", split_axis=0, concat_axis=0, tiled=True).reshape(
        slots_all, columns
    )
    gate_part = jnp.dot(received, gate_proj[0], preferred_element_type=jnp.float32)
    up_part = jnp.dot(received, up_proj[0], preferred_element_type=jnp.float32)
    gate_up = jnp.concatenate([gate_part, up_part], axis=1)
    summed = lax.psum_scatter(gate_up, "dp", scatter_dimension=0, tiled=True)
    summed = lax.optimization_barrier(summed)
    hidden = gather_rows(swiglu(summed), "dp")
    width = columns // n_pipe
    expert_part = jnp.einsum(
        "srf,fpc->psrc",
        hidden.reshape(groups, capacity, -1),
        down_proj[0].reshape(-1, n_pipe, width),
        preferred_element_type=jnp.float32,
    )
    outgoing = expert_part.astype(jnp.bfloat16).reshape(n_pipe * groups, capacity, width)
    arrived = lax.all_to_all(outgoing, ("pipe", "expert"), split_axis=0, concat_axis=0, tiled=True)
    returned = jnp.sum(
        arrived.reshape(n_pipe, groups, capacity, width).astype(jnp.float32), axis=0
    )
    combined = lax.dot_general(
        weighting.reshape(tok_rows, groups, capacity),
        returned,
        (((1, 2), (0, 1)), ((), ())),
        precision=lax.Precision.HIGHEST,
        preferred_element_type=jnp.float32,
    )
    return gather_cols(combined.astype(jnp.bfloat16), "pipe")


def gather_cols(part, axis):
    count = lax.axis_size(axis)
    copies = jnp.broadcast_to(part[None], (count,) + part.shape)
    gathered = lax.all_to_all(copies, axis, split_axis=0, concat_axis=0, tiled=True)
    return jnp.transpose(gathered, (1, 0, 2)).reshape(part.shape[0], count * part.shape[1])

def solution(mesh):
    return jax.shard_map(
        body,
        mesh=mesh,
        in_specs=(
            P("expert", "dp"),
            P("expert", None),
            P("expert", None),
            P("expert", "dp", "pipe"),
            P("expert", "dp", "pipe"),
            P("expert", "pipe", "dp"),
        ),
        out_specs=P("expert", "dp"),
        check_vma=False,
    )
```

```python
import jax
import jax.numpy as jnp
from jax import lax
from jax.sharding import PartitionSpec as P


def swiglu(gate_up):
    middle = gate_up.shape[1] // 2
    return (jax.nn.silu(gate_up[:, :middle]) * gate_up[:, middle:]).astype(jnp.bfloat16)


def gather_rows(part, axis):
    count = lax.axis_size(axis)
    copies = jnp.broadcast_to(part[None], (count,) + part.shape)
    gathered = lax.all_to_all(copies, axis, split_axis=0, concat_axis=0, tiled=True)
    return gathered.reshape((count * part.shape[0],) + part.shape[1:])


def body(tokens, expert_ids, gate_share, gate_proj, up_proj, down_proj):
    tok_rows = tokens.shape[0]
    columns = tokens.shape[1]
    groups = lax.axis_size("expert")
    n_pipe = lax.axis_size("pipe")
    capacity = min(tok_rows, 5 * tok_rows // (2 * groups))
    slots_all = groups * capacity
    choices_flat = expert_ids.reshape(-1)
    onehot = (choices_flat[:, None] == jnp.arange(groups, dtype=jnp.int32)[None, :]).astype(
        jnp.bfloat16
    )
    order = jnp.arange(choices_flat.shape[0], dtype=jnp.int32)
    earlier = (order[None, :] < order[:, None]).astype(jnp.bfloat16)
    before = jnp.dot(earlier, onehot, preferred_element_type=jnp.float32)
    slot_rank = jnp.sum(before * onehot.astype(jnp.float32), axis=1).astype(jnp.int32)
    target = choices_flat * capacity + slot_rank
    placed = (target[:, None] == jnp.arange(slots_all, dtype=jnp.int32)[None, :]).reshape(
        tok_rows, 2, slots_all
    )
    dispatch_map = jnp.sum(placed.astype(jnp.bfloat16), axis=1)
    weighting = jnp.sum(placed.astype(jnp.float32) * gate_share[:, :, None], axis=1)
    outbound = lax.dot_general(
        dispatch_map, tokens, (((0,), (0,)), ((), ())), preferred_element_type=jnp.float32
    )
    outbound = outbound.astype(jnp.bfloat16).reshape(groups, capacity, columns)
    received = lax.all_to_all(outbound, "expert", split_axis=0, concat_axis=0, tiled=True).reshape(
        slots_all, columns
    )
    gate_part = jnp.dot(received, gate_proj[0], preferred_element_type=jnp.float32)
    up_part = jnp.dot(received, up_proj[0], preferred_element_type=jnp.float32)
    gate_up = jnp.concatenate([gate_part, up_part], axis=1)
    summed = lax.psum_scatter(gate_up, "dp", scatter_dimension=0, tiled=True)
    summed = lax.optimization_barrier(summed)
    hidden = gather_rows(swiglu(summed), "dp")
    width = columns // n_pipe
    expert_part = jnp.einsum(
        "srf,fpc->psrc",
        hidden.reshape(groups, capacity, -1),
        down_proj[0].reshape(-1, n_pipe, width),
        preferred_element_type=jnp.float32,
    )
    outgoing = expert_part.astype(jnp.bfloat16).reshape(n_pipe * groups, capacity, width)
    arrived = lax.all_to_all(outgoing, ("pipe", "expert"), split_axis=0, concat_axis=0, tiled=True)
    returned = jnp.sum(
        arrived.reshape(n_pipe, groups, capacity, width).astype(jnp.float32), axis=0
    )
    combined = lax.dot_general(
        weighting.reshape(tok_rows, groups, capacity),
        returned,
        (((1, 2), (0, 1)), ((), ())),
        precision=lax.Precision.HIGHEST,
        preferred_element_type=jnp.float32,
    )
    return gather_cols(combined.astype(jnp.bfloat16), "pipe")


def gather_cols(part, axis):
    count = lax.axis_size(axis)
    copies = jnp.broadcast_to(part[None], (count,) + part.shape)
    gathered = lax.all_to_all(copies, axis, split_axis=0, concat_axis=0, tiled=True)
    return jnp.transpose(gathered, (1, 0, 2)).reshape(part.shape[0], count * part.shape[1])

def solution(mesh):
    return jax.shard_map(
        body,
        mesh=mesh,
        in_specs=(
            P("expert", "dp"),
            P("expert", None),
            P("expert", None),
            P("expert", "dp", "pipe"),
            P("expert", "dp", "pipe"),
            P("expert", "pipe", "dp"),
        ),
        out_specs=P("expert", "dp"),
        check_vma=False,
    )
```

```python
import jax
import jax.numpy as jnp
from jax import lax
from jax.sharding import PartitionSpec as P


def swiglu(gate_up):
    middle = gate_up.shape[1] // 2
    return (jax.nn.silu(gate_up[:, :middle]) * gate_up[:, middle:]).astype(jnp.bfloat16)


def gather_rows(part, axis):
    count = lax.axis_size(axis)
    copies = jnp.broadcast_to(part[None], (count,) + part.shape)
    gathered = lax.all_to_all(copies, axis, split_axis=0, concat_axis=0, tiled=True)
    return gathered.reshape((count * part.shape[0],) + part.shape[1:])


def body(tokens, expert_ids, gate_share, gate_proj, up_proj, down_proj):
    tok_rows = tokens.shape[0]
    columns = tokens.shape[1]
    groups = lax.axis_size("expert")
    n_pipe = lax.axis_size("pipe")
    capacity = min(tok_rows, 5 * tok_rows // (2 * groups))
    slots_all = groups * capacity
    experts = jnp.arange(groups, dtype=jnp.int32)
    first = (expert_ids[:, 0:1] == experts[None, :]).astype(jnp.bfloat16)
    second = (expert_ids[:, 1:2] == experts[None, :]).astype(jnp.bfloat16)
    order = jnp.arange(tok_rows, dtype=jnp.int32)
    earlier = (order[None, :] < order[:, None]).astype(jnp.bfloat16)
    before = jnp.dot(earlier, first + second, preferred_element_type=jnp.float32)
    rank_first = jnp.sum(before * first.astype(jnp.float32), axis=1)
    rank_second = jnp.sum((before + first.astype(jnp.float32)) * second.astype(jnp.float32), axis=1)
    slot_rank = jnp.stack([rank_first, rank_second], axis=1).astype(jnp.int32)
    target = expert_ids * capacity + slot_rank
    placed = target[:, :, None] == jnp.arange(slots_all, dtype=jnp.int32)[None, None, :]
    dispatch_map = jnp.sum(placed.astype(jnp.bfloat16), axis=1)
    weighting = jnp.sum(placed.astype(jnp.float32) * gate_share[:, :, None], axis=1)
    outbound = lax.dot_general(
        dispatch_map, tokens, (((0,), (0,)), ((), ())), preferred_element_type=jnp.float32
    )
    outbound = outbound.astype(jnp.bfloat16).reshape(groups, capacity, columns)
    received = lax.all_to_all(outbound, "expert", split_axis=0, concat_axis=0, tiled=True).reshape(
        slots_all, columns
    )
    gate_part = jnp.dot(received, gate_proj[0], preferred_element_type=jnp.float32)
    up_part = jnp.dot(received, up_proj[0], preferred_element_type=jnp.float32)
    gate_up = jnp.concatenate([gate_part, up_part], axis=1)
    summed = lax.psum_scatter(gate_up, "dp", scatter_dimension=0, tiled=True)
    summed = lax.optimization_barrier(summed)
    hidden = gather_rows(swiglu(summed), "dp")
    width = columns // n_pipe
    expert_part = jnp.einsum(
        "srf,fpc->psrc",
        hidden.reshape(groups, capacity, -1),
        down_proj[0].reshape(-1, n_pipe, width),
        preferred_element_type=jnp.float32,
    )
    outgoing = expert_part.astype(jnp.bfloat16).reshape(n_pipe * groups, capacity, width)
    arrived = lax.all_to_all(outgoing, ("pipe", "expert"), split_axis=0, concat_axis=0, tiled=True)
    returned = jnp.sum(
        arrived.reshape(n_pipe, groups, capacity, width).astype(jnp.float32), axis=0
    )
    combined = lax.dot_general(
        weighting.reshape(tok_rows, groups, capacity),
        returned,
        (((1, 2), (0, 1)), ((), ())),
        precision=lax.Precision.HIGHEST,
        preferred_element_type=jnp.float32,
    )
    return gather_cols(combined.astype(jnp.bfloat16), "pipe")


def gather_cols(part, axis):
    count = lax.axis_size(axis)
    copies = jnp.broadcast_to(part[None], (count,) + part.shape)
    gathered = lax.all_to_all(copies, axis, split_axis=0, concat_axis=0, tiled=True)
    return jnp.transpose(gathered, (1, 0, 2)).reshape(part.shape[0], count * part.shape[1])

def solution(mesh):
    return jax.shard_map(
        body,
        mesh=mesh,
        in_specs=(
            P("expert", "dp"),
            P("expert", None),
            P("expert", None),
            P("expert", "dp", "pipe"),
            P("expert", "dp", "pipe"),
            P("expert", "pipe", "dp"),
        ),
        out_specs=P("expert", "dp"),
        check_vma=False,
    )
```
